32 devices in a mesh: tiles: 2 (over y), view: 4 (over z), gz: 4 (over x, core).
Axes of the slice: x: 2, y: 2, z: 4, core: 2. Of those that a mesh axis runs over, the one named last changes fastest.
Arguments:
- images: float32 [4, 128, 128, 256], P('view', ('tiles', 'gz')), parts along dimension 1, may hold values from 0.2 to 160
- first_guess: float32 [128, 128, 256], P(('tiles', 'gz')), parts along dimension 0, may hold values from 0.5 to 1.5
- axial_taps: float32 [4, 3, 15], P('view'), may hold values from 0 to 1
- row_taps: float32 [4, 3, 15], P('view'), may hold values from 0 to 1
- column_taps: float32 [4, 3, 15], P('view'), may hold values from 0 to 1
Outputs:
- refined: float32 [128, 128, 256], P(('tiles', 'gz')), parts along dimension 0
The draws below stay inside these ranges and needn't reach their ends.
There are 2 independent parts, one for each index of `tiles`. The reference program is written for one: setup_inputs(seed, part) draws one part's arguments, and reference() takes and returns one part's arrays. A program takes and returns all parts, laid end to end along the dimension named above; an argument that names none is the same for every part. Nothing has to cross between parts.
All inputs are finite; a program needn't handle non-finite values.
Results may differ from the reference program's by a relative error of at most 0.000096.
Values sent between devices are 32-bit elements; how exact they have to be, the bound alone decides.
No kernel may reach another device: no remote copies, remote signals or barrier semaphores. Data moves between devices by JAX's collectives and lax.ppermute only.
A program may use at most 64 MiB of HBM per device.

```python
import math
import jax
import jax.numpy as jnp

PLANE_Y = 128
PLANE_X = 256
RANK = 3
TAPS = 15
ITERS = 2
VIEWS = 4
ZTOT = 64


def tap_profile(key, narrowest, widest):
    spreads = jnp.exp(jax.random.uniform(jax.random.fold_in(key, 1), (VIEWS, RANK, 1), jnp.float32, math.log(narrowest), math.log(widest)))
    offsets = jax.random.uniform(jax.random.fold_in(key, 2), (VIEWS, RANK, 1), jnp.float32, -1.0, 1.0)
    roughness = jax.random.uniform(jax.random.fold_in(key, 3), (VIEWS, RANK, TAPS), jnp.float32, 0.6, 1.4)
    position = jnp.arange(TAPS, dtype=jnp.float32)[None, None, :] - (TAPS - 1) / 2.0 - offsets
    profile = jnp.exp(-position * position / (2.0 * spreads * spreads)) / (spreads * 2.5066283)
    return (roughness * profile).astype(jnp.float32)


def draw_axial_taps(key, part):
    return tap_profile(jax.random.fold_in(key, 21), 1.0, 4.0)


def draw_row_taps(key, part):
    return tap_profile(jax.random.fold_in(key, 22), 0.7, 2.5)


def draw_column_taps(key, part):
    return tap_profile(jax.random.fold_in(key, 23), 0.7, 2.5)


def draw_images(key, part):
    full_shape = (VIEWS, ZTOT, PLANE_Y, PLANE_X)
    volume = (ZTOT, PLANE_Y, PLANE_X)
    background = jax.random.uniform(jax.random.fold_in(key, 31), full_shape, jnp.float32, 0.2, 2.0)
    brightness = jax.random.uniform(jax.random.fold_in(key, 33), volume, jnp.float32, 40.0, 120.0)
    beads = jax.random.bernoulli(jax.random.fold_in(key, 32), 0.005, volume).astype(jnp.float32)
    view_gain = jax.random.uniform(jax.random.fold_in(key, 34), (VIEWS, 1, 1, 1), jnp.float32, 0.7, 1.3)
    return (background + view_gain * (beads * brightness)[None]).astype(jnp.float32)


def steps_of(stream_key, shape, shards, low, top_value):
    loudness, own = 1.0, jax.random.fold_in(stream_key, 6)
    for axis_at, parts in shards:
        heights = jnp.exp(jax.random.uniform(jax.random.fold_in(own, axis_at), (parts,), jnp.float32, low / len(shards), top_value / len(shards)))
        loudness = loudness * jnp.repeat(heights, shape[axis_at] // parts).reshape([-1 if axis == axis_at else 1 for axis in range(len(shape))])
    return loudness


def setup_inputs(seed: int = 0, part: int = 0) -> dict:
    key_list = jax.random.split(jax.random.key(seed), 6)
    part_splits = jax.random.split(jax.random.fold_in(key_list[5], part), 6)
    return {
        "images": draw_images(jax.random.fold_in(jax.random.fold_in(key_list[5], part), 71), part),
        "first_guess": jnp.clip(0.5 + 1.0 * jax.random.uniform(part_splits[1], (ZTOT, PLANE_Y, PLANE_X), jnp.float32) ** steps_of(part_splits[1], (ZTOT, PLANE_Y, PLANE_X), ((0, 4),), -0.2, 0.2), 0.5, 1.5),
        "axial_taps": draw_axial_taps(jax.random.fold_in(key_list[5], 71), part),
        "row_taps": draw_row_taps(jax.random.fold_in(key_list[5], 71), part),
        "column_taps": draw_column_taps(jax.random.fold_in(key_list[5], 71), part),
    }


def shifted_sum(field, kernel_taps, along, forward):
    half = (TAPS - 1) // 2
    widths = [(0, 0), (0, 0), (0, 0)]
    widths[along] = (half, half)
    padded = jnp.pad(field, widths)
    length = field.shape[along]
    result = jnp.zeros_like(field)
    for tap_index in range(TAPS):
        offset = tap_index if forward else TAPS - 1 - tap_index
        result = result + kernel_taps[tap_index] * jax.lax.slice_in_dim(padded, offset, offset + length, axis=along)
    return result


def blur_view(field, axial, rows, columns, forward):
    result = jnp.zeros_like(field)
    for term in range(RANK):
        section = shifted_sum(field, axial[term], 0, forward)
        section = shifted_sum(section, rows[term], 1, forward)
        section = shifted_sum(section, columns[term], 2, forward)
        result = result + section
    return result


def reference(images, first_guess, axial_taps, row_taps, column_taps):
    estimate = first_guess
    for iteration in range(ITERS):
        logsum = jnp.zeros_like(estimate)
        for view_index in range(VIEWS):
            blurred = blur_view(estimate, axial_taps[view_index], row_taps[view_index], column_taps[view_index], True)
            ratio = images[view_index] / blurred
            correction = blur_view(ratio, axial_taps[view_index], row_taps[view_index], column_taps[view_index], False)
            logsum = logsum + jnp.log(correction)
        estimate = estimate * jnp.exp(logsum / VIEWS)
    return estimate
```

```python
import jax
import jax.numpy as jnp
from jax import lax
from jax.sharding import PartitionSpec as P

PLANE_Y = 128
PLANE_X = 256
ITERS = 2
PREC = lax.Precision.HIGH


def padded_2(x, sides, width):
    for axis, dim in sides:
        peers, length = (lax.axis_size(axis), x.shape[dim])
        up = [(i, (i + 1) % peers) for i in range(peers - 1)]
        down = [(j, i) for i, j in up]
        last = lax.slice_in_dim(x, length - width, length, axis=dim)
        initial = lax.slice_in_dim(x, 0, width, axis=dim)
        before = lax.ppermute(last, axis, up)
        after = lax.ppermute(initial, axis, down)
        x = jnp.concatenate([before, x, after], axis=dim)
    return x


def band_table(kernel_taps, length_in, length_out, offset, forward):
    inner = lax.broadcasted_iota(jnp.int32, (length_in, length_out), 0)
    outer = lax.broadcasted_iota(jnp.int32, (length_in, length_out), 1)
    if forward:
        index_diff = inner - outer + offset
    else:
        index_diff = outer - inner + offset
    tap_ids = lax.broadcasted_iota(jnp.int32, (kernel_taps.shape[1], length_in, length_out), 0)
    onehot = (index_diff[None, :, :] == tap_ids).astype(jnp.float32)
    return jnp.einsum("rk,kio->rio", kernel_taps, onehot, precision=lax.Precision.HIGHEST)


def make_tables(axial, rows, columns, slab_planes, forward):
    tap_count = axial.shape[1]
    half = (tap_count - 1) // 2
    plane_rows = PLANE_Y
    plane_columns = PLANE_X
    axial_table = band_table(
        axial, slab_planes + 2 * half, slab_planes, 0 if forward else 2 * half, forward
    )
    row_table = band_table(rows, plane_rows, plane_rows, half, forward)
    column_table = band_table(columns, plane_columns, plane_columns, half, forward)
    return (axial_table, row_table, column_table)


def apply_blur(padded, tables):
    axial_table, row_table, column_table = tables
    axial_pass = jnp.einsum("rqw,qyx->rwyx", axial_table, padded, precision=PREC)
    row_pass = jnp.einsum("rwyx,ryv->rwvx", axial_pass, row_table, precision=PREC)
    return jnp.einsum("rwvx,rxu->wvu", row_pass, column_table, precision=PREC)


def body(images, first_guess, axial_taps, row_taps, column_taps):
    recorded = images[0]
    slab_planes = recorded.shape[0]
    half = (axial_taps.shape[2] - 1) // 2
    view_count = lax.axis_size("view") * images.shape[0]
    forward_tables = make_tables(axial_taps[0], row_taps[0], column_taps[0], slab_planes, True)
    adjoint_tables = make_tables(axial_taps[0], row_taps[0], column_taps[0], slab_planes, False)
    estimate = first_guess
    for iteration in range(ITERS):
        padded_estimate = padded_2(estimate, (("gz", 0),), half)
        blurred = apply_blur(padded_estimate, forward_tables)
        ratio = recorded / blurred
        padded_ratio = padded_2(ratio, (("gz", 0),), half)
        correction = apply_blur(padded_ratio, adjoint_tables)
        log_terms = jnp.log(correction)
        logsum = lax.psum(log_terms, "view")
        estimate = estimate * jnp.exp(logsum / view_count)
    return estimate


def solution(mesh):
    in_specs = (
        P("view", ("tiles", "gz"), None, None),
        P(("tiles", "gz"), None, None),
        P("view", None, None),
        P("view", None, None),
        P("view", None, None),
    )
    out_specs = P(("tiles", "gz"), None, None)
    return jax.shard_map(body, mesh=mesh, in_specs=in_specs, out_specs=out_specs, check_vma=False)
```

```python
import functools

import jax
import jax.numpy as jnp
from jax import lax
from jax.sharding import PartitionSpec as P

PLANE_Y = 128
PLANE_X = 256
ITERS = 2
PREC = lax.Precision.HIGH
PIECES = 8


def padded_2(x, sides, width):
    for axis, dim in sides:
        peers, length = (lax.axis_size(axis), x.shape[dim])
        up = [(i, (i + 1) % peers) for i in range(peers - 1)]
        down = [(j, i) for i, j in up]
        last = lax.slice_in_dim(x, length - width, length, axis=dim)
        initial = lax.slice_in_dim(x, 0, width, axis=dim)
        before = lax.ppermute(last, axis, up)
        after = lax.ppermute(initial, axis, down)
        x = jnp.concatenate([before, x, after], axis=dim)
    return x


def band_table(kernel_taps, length_in, length_out, offset, forward):
    inner = lax.broadcasted_iota(jnp.int32, (length_in, length_out), 0)
    outer = lax.broadcasted_iota(jnp.int32, (length_in, length_out), 1)
    if forward:
        index_diff = inner - outer + offset
    else:
        index_diff = outer - inner + offset
    tap_ids = lax.broadcasted_iota(jnp.int32, (kernel_taps.shape[1], length_in, length_out), 0)
    onehot = (index_diff[None, :, :] == tap_ids).astype(jnp.float32)
    return jnp.einsum("rk,kio->rio", kernel_taps, onehot, precision=lax.Precision.HIGHEST)


def make_tables(axial, rows, columns, slab_planes, forward):
    tap_count = axial.shape[1]
    half = (tap_count - 1) // 2
    plane_rows = PLANE_Y
    plane_columns = PLANE_X
    axial_table = band_table(
        axial, slab_planes + 2 * half, slab_planes, 0 if forward else 2 * half, forward
    )
    row_table = band_table(rows, plane_rows, plane_rows, half, forward)
    column_table = band_table(columns, plane_columns, plane_columns, half, forward)
    return (axial_table, row_table, column_table)


def apply_blur(padded, tables, pieces=1):
    axial_table, row_table, column_table = tables
    axial_pass = jnp.einsum("rqw,qyx->rwyx", axial_table, padded, precision=PREC)
    row_pass = jnp.einsum("rwyx,ryv->rwvx", axial_pass, row_table, precision=PREC)
    if pieces == 1:
        return jnp.einsum("rwvx,rxu->wvu", row_pass, column_table, precision=PREC)
    width = row_pass.shape[1] // pieces
    return [
        jnp.einsum("rwvx,rxu->wvu", row_pass[:, i * width:(i + 1) * width], column_table, precision=PREC)
        for i in range(pieces)
    ]


def line_psum(x, axis):
    n = lax.axis_size(axis)
    if n == 1:
        return x
    me = lax.axis_index(axis)
    m = n // 2
    steps = max(m - 1, n - m - 1)
    acc = x
    for s in range(steps):
        pairs = []
        if s < m - 1:
            pairs.append((s, s + 1))
        if s < n - m - 1:
            pairs.append((n - 1 - s, n - 2 - s))
        acc = acc + lax.ppermute(acc, axis, pairs)
    acc = acc + lax.ppermute(acc, axis, [(m - 1, m), (m, m - 1)])
    for s in range(steps):
        pairs, receivers = [], []
        if s < m - 1:
            pairs.append((m - 1 - s, m - 2 - s))
            receivers.append(m - 2 - s)
        if s < n - m - 1:
            pairs.append((m + s, m + 1 + s))
            receivers.append(m + 1 + s)
        got = lax.ppermute(acc, axis, pairs)
        hit = functools.reduce(jnp.logical_or, [me == r for r in receivers])
        acc = jnp.where(hit, got, acc)
    return acc


def body(images, first_guess, axial_taps, row_taps, column_taps):
    recorded = images[0]
    slab_planes = recorded.shape[0]
    half = (axial_taps.shape[2] - 1) // 2
    view_count = lax.axis_size("view") * images.shape[0]
    forward_tables = make_tables(axial_taps[0], row_taps[0], column_taps[0], slab_planes, True)
    adjoint_tables = make_tables(axial_taps[0], row_taps[0], column_taps[0], slab_planes, False)
    estimate = first_guess
    for iteration in range(ITERS):
        padded_estimate = padded_2(estimate, (("gz", 0),), half)
        blurred = apply_blur(padded_estimate, forward_tables)
        ratio = recorded / blurred
        padded_ratio = padded_2(ratio, (("gz", 0),), half)
        pieces = PIECES if slab_planes % PIECES == 0 else 1
        corrections = apply_blur(padded_ratio, adjoint_tables, pieces)
        if pieces == 1:
            corrections = [corrections]
        width = slab_planes // pieces
        updated = []
        for i, correction in enumerate(corrections):
            logsum = line_psum(jnp.log(correction), "view")
            part = estimate[i * width:(i + 1) * width]
            updated.append(part * jnp.exp(logsum / view_count))
        estimate = jnp.concatenate(updated, axis=0)
    return estimate


def solution(mesh):
    in_specs = (
        P("view", ("tiles", "gz"), None, None),
        P(("tiles", "gz"), None, None),
        P("view", None, None),
        P("view", None, None),
        P("view", None, None),
    )
    out_specs = P(("tiles", "gz"), None, None)
    return jax.shard_map(body, mesh=mesh, in_specs=in_specs, out_specs=out_specs, check_vma=False)
```

```python
import jax
import jax.numpy as jnp
from jax import lax
from jax.sharding import PartitionSpec as P

ITERS = 2
PREC = lax.Precision.HIGH
PIECES = 2


def padded_2(x, sides, width):
    for axis, dim in sides:
        peers, length = (lax.axis_size(axis), x.shape[dim])
        up = [(i, (i + 1) % peers) for i in range(peers - 1)]
        down = [(j, i) for i, j in up]
        last = lax.slice_in_dim(x, length - width, length, axis=dim)
        initial = lax.slice_in_dim(x, 0, width, axis=dim)
        before = lax.ppermute(last, axis, up)
        after = lax.ppermute(initial, axis, down)
        x = jnp.concatenate([before, x, after], axis=dim)
    return x


def band_table(kernel_taps, length_in, length_out, offset, forward):
    inner = lax.broadcasted_iota(jnp.int32, (length_in, length_out), 0)
    outer = lax.broadcasted_iota(jnp.int32, (length_in, length_out), 1)
    if forward:
        index_diff = inner - outer + offset
    else:
        index_diff = outer - inner + offset
    tap_ids = lax.broadcasted_iota(jnp.int32, (kernel_taps.shape[1], length_in, length_out), 0)
    onehot = (index_diff[None, :, :] == tap_ids).astype(jnp.float32)
    return jnp.einsum("rk,kio->rio", kernel_taps, onehot, precision=lax.Precision.HIGHEST)


def apply_blur(padded, axial_table, row_table, column_table):
    axial_pass = jnp.einsum("rqw,qyx->rwyx", axial_table, padded, precision=PREC)
    row_pass = jnp.einsum("rwyx,ryv->rwvx", axial_pass, row_table, precision=PREC)
    return jnp.einsum("rwvx,rxu->wvu", row_pass, column_table, precision=PREC)


def widen(window, width, rows):
    return (max(0, window[0] - width), min(rows, window[1] + width))


def body(images, first_guess, axial_taps, row_taps, column_taps):
    recorded = images[0]
    planes, rows, columns = recorded.shape
    half = (axial_taps.shape[2] - 1) // 2
    margin = -(-half // 8) * 8
    view_count = lax.axis_size("view") * images.shape[0]
    axial, row_k, column_k = axial_taps[0], row_taps[0], column_taps[0]
    axial_fwd = band_table(axial, planes + 2 * half, planes, 0, True)
    axial_adj = band_table(axial, planes + 2 * half, planes, 2 * half, False)
    column_fwd = band_table(column_k, columns, columns, half, True)
    column_adj = band_table(column_k, columns, columns, half, False)
    pieces = PIECES if rows % (8 * PIECES) == 0 else 1
    step = rows // pieces
    windows = []
    estimates = []
    for p in range(pieces):
        est_win = [None] * (ITERS + 1)
        ratio_win = [None] * ITERS
        est_win[ITERS] = (p * step, (p + 1) * step)
        for it in reversed(range(ITERS)):
            ratio_win[it] = widen(est_win[it + 1], margin, rows)
            est_win[it] = widen(ratio_win[it], margin, rows)
        windows.append((est_win, ratio_win))
        estimates.append(first_guess[:, est_win[0][0]:est_win[0][1]])
    previous = None
    for it in range(ITERS):
        for p in range(pieces):
            est_win, ratio_win = windows[p]
            estimate = estimates[p]
            (ei, ej), (ri, rj), (ni, nj) = est_win[it], ratio_win[it], est_win[it + 1]
            row_fwd = band_table(row_k, ej - ei, rj - ri, ei - ri + half, True)
            row_adj = band_table(row_k, rj - ri, nj - ni, ni - ri + half, False)
            padded_estimate = padded_2(estimate, (("gz", 0),), half)
            blurred = apply_blur(padded_estimate, axial_fwd, row_fwd, column_fwd)
            ratio = recorded[:, ri:rj] / blurred
            padded_ratio = padded_2(ratio, (("gz", 0),), half)
            correction = apply_blur(padded_ratio, axial_adj, row_adj, column_adj)
            log_terms = jnp.log(correction)
            if previous is not None:
                log_terms, _ = lax.optimization_barrier((log_terms, previous))
            logsum = lax.psum(log_terms, "view")
            previous = logsum
            estimates[p] = estimate[:, ni - ei:nj - ei] * jnp.exp(logsum / view_count)
    outputs = estimates
    return jnp.concatenate(outputs, axis=1) if pieces > 1 else outputs[0]


def solution(mesh):
    in_specs = (
        P("view", ("tiles", "gz"), None, None),
        P(("tiles", "gz"), None, None),
        P("view", None, None),
        P("view", None, None),
        P("view", None, None),
    )
    out_specs = P(("tiles", "gz"), None, None)
    return jax.shard_map(body, mesh=mesh, in_specs=in_specs, out_specs=out_specs, check_vma=False)
```

```python
import jax
import jax.numpy as jnp
from jax import lax
from jax.sharding import PartitionSpec as P

ITERS = 2
PREC = lax.Precision.HIGH
PIECES = 2


def padded_2(x, sides, width):
    for axis, dim in sides:
        peers, length = (lax.axis_size(axis), x.shape[dim])
        up = [(i, (i + 1) % peers) for i in range(peers - 1)]
        down = [(j, i) for i, j in up]
        last = lax.slice_in_dim(x, length - width, length, axis=dim)
        initial = lax.slice_in_dim(x, 0, width, axis=dim)
        before = lax.ppermute(last, axis, up)
        after = lax.ppermute(initial, axis, down)
        x = jnp.concatenate([before, x, after], axis=dim)
    return x


def band_table(kernel_taps, length_in, length_out, offset, forward):
    inner = lax.broadcasted_iota(jnp.int32, (length_in, length_out), 0)
    outer = lax.broadcasted_iota(jnp.int32, (length_in, length_out), 1)
    if forward:
        index_diff = inner - outer + offset
    else:
        index_diff = outer - inner + offset
    tap_ids = lax.broadcasted_iota(jnp.int32, (kernel_taps.shape[1], length_in, length_out), 0)
    onehot = (index_diff[None, :, :] == tap_ids).astype(jnp.float32)
    return jnp.einsum("rk,kio->rio", kernel_taps, onehot, precision=lax.Precision.HIGHEST)


def apply_blur(padded, axial_table, row_table, column_table):
    axial_pass = jnp.einsum("rqw,qyx->rwyx", axial_table, padded, precision=PREC)
    row_pass = jnp.einsum("rwyx,ryv->rwvx", axial_pass, row_table, precision=PREC)
    return jnp.einsum("rwvx,rxu->wvu", row_pass, column_table, precision=PREC)


def widen(window, width, rows):
    return (max(0, window[0] - width), min(rows, window[1] + width))


def body(images, first_guess, axial_taps, row_taps, column_taps):
    recorded = images[0]
    planes, rows, columns = recorded.shape
    half = (axial_taps.shape[2] - 1) // 2
    margin = -(-half // 8) * 8
    view_count = lax.axis_size("view") * images.shape[0]
    axial, row_k, column_k = axial_taps[0], row_taps[0], column_taps[0]
    axial_fwd = band_table(axial, planes + 2 * half, planes, 0, True)
    axial_adj = band_table(axial, planes + 2 * half, planes, 2 * half, False)
    column_fwd = band_table(column_k, columns, columns, half, True)
    column_adj = band_table(column_k, columns, columns, half, False)
    pieces = PIECES if rows % (8 * PIECES) == 0 else 1
    step = rows // pieces
    needed = [[None] * (ITERS + 1) for _ in range(pieces)]
    for p in range(pieces):
        needed[p][ITERS] = (p * step, (p + 1) * step)
        for it in reversed(range(ITERS)):
            needed[p][it] = widen(needed[p][it + 1], 2 * margin, rows)
    made = [[(needed[p][0], None) for p in range(pieces)]]
    previous_log = None
    previous_sum = None
    for it in range(ITERS):
        made.append([])
        done_to = 0
        for p in range(pieces):
            target = needed[p][it + 1]
            ni, nj = (target[0], target[1]) if it + 1 == ITERS else (max(target[0], done_to), target[1])
            done_to = nj
            ri, rj = widen((ni, nj), margin, rows)
            ei, ej = widen((ri, rj), margin, rows)
            if it == 0:
                estimate = first_guess[:, ei:ej]
            else:
                parts = []
                for (ci, cj), values in made[it]:
                    lo, hi = max(ci, ei), min(cj, ej)
                    if lo < hi:
                        parts.append(values[:, lo - ci:hi - ci])
                estimate = jnp.concatenate(parts, axis=1) if len(parts) > 1 else parts[0]
            if previous_log is not None:
                estimate, _ = lax.optimization_barrier((estimate, previous_log))
            row_fwd = band_table(row_k, ej - ei, rj - ri, ei - ri + half, True)
            row_adj = band_table(row_k, rj - ri, nj - ni, ni - ri + half, False)
            padded_estimate = padded_2(estimate, (("gz", 0),), half)
            blurred = apply_blur(padded_estimate, axial_fwd, row_fwd, column_fwd)
            ratio = recorded[:, ri:rj] / blurred
            padded_ratio = padded_2(ratio, (("gz", 0),), half)
            correction = apply_blur(padded_ratio, axial_adj, row_adj, column_adj)
            log_terms = jnp.log(correction)
            previous_log = log_terms
            if previous_sum is not None:
                log_terms, _ = lax.optimization_barrier((log_terms, previous_sum))
            logsum = lax.psum(log_terms, "view")
            previous_sum = logsum
            updated = estimate[:, ni - ei:nj - ei] * jnp.exp(logsum / view_count)
            made[it + 1].append(((ni, nj), updated))
    outputs = [values for _, values in made[ITERS]]
    return jnp.concatenate(outputs, axis=1) if pieces > 1 else outputs[0]


def solution(mesh):
    in_specs = (
        P("view", ("tiles", "gz"), None, None),
        P(("tiles", "gz"), None, None),
        P("view", None, None),
        P("view", None, None),
        P("view", None, None),
    )
    out_specs = P(("tiles", "gz"), None, None)
    return jax.shard_map(body, mesh=mesh, in_specs=in_specs, out_specs=out_specs, check_vma=False)
```

```python
import jax
import jax.numpy as jnp
from jax import lax
from jax.sharding import PartitionSpec as P

ITERS = 2
PREC = lax.Precision.HIGH
PIECES = 2


def padded_2(x, sides, width):
    for axis, dim in sides:
        peers, length = (lax.axis_size(axis), x.shape[dim])
        up = [(i, (i + 1) % peers) for i in range(peers - 1)]
        down = [(j, i) for i, j in up]
        last = lax.slice_in_dim(x, length - width, length, axis=dim)
        initial = lax.slice_in_dim(x, 0, width, axis=dim)
        before = lax.ppermute(last, axis, up)
        after = lax.ppermute(initial, axis, down)
        x = jnp.concatenate([before, x, after], axis=dim)
    return x


def band_table(kernel_taps, length_in, length_out, offset, forward):
    inner = lax.broadcasted_iota(jnp.int32, (length_in, length_out), 0)
    outer = lax.broadcasted_iota(jnp.int32, (length_in, length_out), 1)
    if forward:
        index_diff = inner - outer + offset
    else:
        index_diff = outer - inner + offset
    tap_ids = lax.broadcasted_iota(jnp.int32, (kernel_taps.shape[1], length_in, length_out), 0)
    onehot = (index_diff[None, :, :] == tap_ids).astype(jnp.float32)
    return jnp.einsum("rk,kio->rio", kernel_taps, onehot, precision=lax.Precision.HIGHEST)


def apply_blur(padded, axial_table, row_table, column_table):
    axial_pass = jnp.einsum("rqw,qyx->rwyx", axial_table, padded, precision=PREC)
    row_pass = jnp.einsum("rwyx,ryv->rwvx", axial_pass, row_table, precision=PREC)
    return jnp.einsum("rwvx,rxu->wvu", row_pass, column_table, precision=PREC)


def widen(window, width, rows):
    return (max(0, window[0] - width), min(rows, window[1] + width))


def body(images, first_guess, axial_taps, row_taps, column_taps):
    recorded = images[0]
    planes, rows, columns = recorded.shape
    half = (axial_taps.shape[2] - 1) // 2
    margin = -(-half // 8) * 8
    view_count = lax.axis_size("view") * images.shape[0]
    axial, row_k, column_k = axial_taps[0], row_taps[0], column_taps[0]
    axial_fwd = band_table(axial, planes + 2 * half, planes, 0, True)
    axial_adj = band_table(axial, planes + 2 * half, planes, 2 * half, False)
    column_fwd = band_table(column_k, columns, columns, half, True)
    column_adj = band_table(column_k, columns, columns, half, False)
    pieces = PIECES if rows % (8 * PIECES) == 0 else 1
    step = rows // pieces
    needed = [[None] * (ITERS + 1) for _ in range(pieces)]
    for p in range(pieces):
        needed[p][ITERS] = (p * step, (p + 1) * step)
        for it in reversed(range(ITERS)):
            needed[p][it] = widen(needed[p][it + 1], 2 * margin, rows)
    made = [[(needed[p][0], None) for p in range(pieces)]]
    previous_log = None
    previous_sum = None
    for it in range(ITERS):
        made.append([])
        done_to = 0
        for p in range(pieces):
            target = needed[p][it + 1]
            ni, nj = (target[0], target[1]) if it + 1 == ITERS else (max(target[0], done_to), target[1])
            done_to = nj
            ri, rj = widen((ni, nj), margin, rows)
            ei, ej = widen((ri, rj), margin, rows)
            if it == 0:
                estimate = first_guess[:, ei:ej]
            else:
                parts = []
                for (ci, cj), values in made[it]:
                    lo, hi = max(ci, ei), min(cj, ej)
                    if lo < hi:
                        parts.append(values[:, lo - ci:hi - ci])
                estimate = jnp.concatenate(parts, axis=1) if len(parts) > 1 else parts[0]
            if previous_log is not None:
                estimate, _ = lax.optimization_barrier((estimate, previous_log))
            row_fwd = band_table(row_k, ej - ei, rj - ri, ei - ri + half, True)
            row_adj = band_table(row_k, rj - ri, nj - ni, ni - ri + half, False)
            padded_estimate = padded_2(estimate, (("gz", 0),), half)
            blurred = apply_blur(padded_estimate, axial_fwd, row_fwd, column_fwd)
            ratio = recorded[:, ri:rj] / blurred
            padded_ratio = padded_2(ratio, (("gz", 0),), half)
            correction = apply_blur(padded_ratio, axial_adj, row_adj, column_adj)
            log_terms = jnp.log(correction)
            previous_log = log_terms
            if previous_sum is not None:
                log_terms, _ = lax.optimization_barrier((log_terms, previous_sum))
            if planes % lax.axis_size("view") == 0:
                part_sum = lax.psum_scatter(log_terms, "view", scatter_dimension=0, tiled=True)
                logsum = lax.all_gather(part_sum, "view", axis=0, tiled=True)
            else:
                logsum = lax.psum(log_terms, "view")
            previous_sum = logsum
            updated = estimate[:, ni - ei:nj - ei] * jnp.exp(logsum / view_count)
            made[it + 1].append(((ni, nj), updated))
    outputs = [values for _, values in made[ITERS]]
    return jnp.concatenate(outputs, axis=1) if pieces > 1 else outputs[0]


def solution(mesh):
    in_specs = (
        P("view", ("tiles", "gz"), None, None),
        P(("tiles", "gz"), None, None),
        P("view", None, None),
        P("view", None, None),
        P("view", None, None),
    )
    out_specs = P(("tiles", "gz"), None, None)
    return jax.shard_map(body, mesh=mesh, in_specs=in_specs, out_specs=out_specs, check_vma=False)
```

```python
import jax
import jax.numpy as jnp
from jax import lax
from jax.sharding import PartitionSpec as P

ITERS = 2
PREC = lax.Precision.HIGH
PIECES = 2


def padded_2(x, sides, width):
    for axis, dim in sides:
        peers, length = (lax.axis_size(axis), x.shape[dim])
        up = [(i, (i + 1) % peers) for i in range(peers - 1)]
        down = [(j, i) for i, j in up]
        last = lax.slice_in_dim(x, length - width, length, axis=dim)
        initial = lax.slice_in_dim(x, 0, width, axis=dim)
        before = lax.ppermute(last, axis, up)
        after = lax.ppermute(initial, axis, down)
        x = jnp.concatenate([before, x, after], axis=dim)
    return x


def band_table(kernel_taps, length_in, length_out, offset, forward):
    inner = lax.broadcasted_iota(jnp.int32, (length_in, length_out), 0)
    outer = lax.broadcasted_iota(jnp.int32, (length_in, length_out), 1)
    if forward:
        index_diff = inner - outer + offset
    else:
        index_diff = outer - inner + offset
    tap_ids = lax.broadcasted_iota(jnp.int32, (kernel_taps.shape[1], length_in, length_out), 0)
    onehot = (index_diff[None, :, :] == tap_ids).astype(jnp.float32)
    return jnp.einsum("rk,kio->rio", kernel_taps, onehot, precision=lax.Precision.HIGHEST)


def apply_blur(padded, axial_table, row_table, column_table):
    axial_pass = jnp.einsum("rqw,qyx->rwyx", axial_table, padded, precision=PREC)
    row_pass = jnp.einsum("rwyx,ryv->rwvx", axial_pass, row_table, precision=PREC)
    return jnp.einsum("rwvx,rxu->wvu", row_pass, column_table, precision=PREC)


def widen(window, width, rows):
    return (max(0, window[0] - width), min(rows, window[1] + width))


def body(images, first_guess, axial_taps, row_taps, column_taps):
    recorded = images[0]
    planes, rows, columns = recorded.shape
    half = (axial_taps.shape[2] - 1) // 2
    margin = -(-half // 8) * 8
    view_count = lax.axis_size("view") * images.shape[0]
    axial, row_k, column_k = axial_taps[0], row_taps[0], column_taps[0]
    axial_fwd = band_table(axial, planes + 2 * half, planes, 0, True)
    axial_adj = band_table(axial, planes + 2 * half, planes, 2 * half, False)
    column_fwd = band_table(column_k, columns, columns, half, True)
    column_adj = band_table(column_k, columns, columns, half, False)
    pieces = PIECES if rows % (8 * PIECES) == 0 else 1
    step = rows // pieces
    needed = [[None] * (ITERS + 1) for _ in range(pieces)]
    for p in range(pieces):
        needed[p][ITERS] = (p * step, (p + 1) * step)
        for it in reversed(range(ITERS)):
            needed[p][it] = widen(needed[p][it + 1], 2 * margin, rows)
    made = [[(needed[p][0], None) for p in range(pieces)]]
    previous_log = None
    previous_sum = None
    for it in range(ITERS):
        made.append([])
        done_to = 0
        for p in range(pieces):
            target = needed[p][it + 1]
            ni, nj = (target[0], target[1]) if it + 1 == ITERS else (max(target[0], done_to), target[1])
            done_to = nj
            ri, rj = widen((ni, nj), margin, rows)
            ei, ej = widen((ri, rj), margin, rows)
            if it == 0:
                estimate = first_guess[:, ei:ej]
            else:
                parts = []
                for (ci, cj), values in made[it]:
                    lo, hi = max(ci, ei), min(cj, ej)
                    if lo < hi:
                        parts.append(values[:, lo - ci:hi - ci])
                estimate = jnp.concatenate(parts, axis=1) if len(parts) > 1 else parts[0]
            if previous_log is not None:
                estimate, _ = lax.optimization_barrier((estimate, previous_log))
            row_fwd = band_table(row_k, ej - ei, rj - ri, ei - ri + half, True)
            row_adj = band_table(row_k, rj - ri, nj - ni, ni - ri + half, False)
            padded_estimate = padded_2(estimate, (("gz", 0),), half)
            blurred = apply_blur(padded_estimate, axial_fwd, row_fwd, column_fwd)
            ratio = recorded[:, ri:rj] / blurred
            padded_ratio = padded_2(ratio, (("gz", 0),), half)
            correction = apply_blur(padded_ratio, axial_adj, row_adj, column_adj)
            log_terms = jnp.log(correction)
            previous_log = log_terms
            if previous_sum is not None:
                log_terms, _ = lax.optimization_barrier((log_terms, previous_sum))
            last = it + 1 == ITERS and p + 1 == pieces
            if planes % lax.axis_size("view") == 0 and log_terms.size >= (1 << 18) and not last:
                part_sum = lax.psum_scatter(log_terms, "view", scatter_dimension=0, tiled=True)
                logsum = lax.all_gather(part_sum, "view", axis=0, tiled=True)
            else:
                logsum = lax.psum(log_terms, "view")
            previous_sum = logsum
            updated = estimate[:, ni - ei:nj - ei] * jnp.exp(logsum / view_count)
            made[it + 1].append(((ni, nj), updated))
    outputs = [values for _, values in made[ITERS]]
    return jnp.concatenate(outputs, axis=1) if pieces > 1 else outputs[0]


def solution(mesh):
    in_specs = (
        P("view", ("tiles", "gz"), None, None),
        P(("tiles", "gz"), None, None),
        P("view", None, None),
        P("view", None, None),
        P("view", None, None),
    )
    out_specs = P(("tiles", "gz"), None, None)
    return jax.shard_map(body, mesh=mesh, in_specs=in_specs, out_specs=out_specs, check_vma=False)
```

```python
import jax
import jax.numpy as jnp
from jax import lax
from jax.sharding import PartitionSpec as P

ITERS = 2
PREC = lax.Precision.HIGH
PIECES = 2


def padded_2(x, sides, width):
    for axis, dim in sides:
        peers, length = (lax.axis_size(axis), x.shape[dim])
        up = [(i, (i + 1) % peers) for i in range(peers - 1)]
        down = [(j, i) for i, j in up]
        last = lax.slice_in_dim(x, length - width, length, axis=dim)
        initial = lax.slice_in_dim(x, 0, width, axis=dim)
        before = lax.ppermute(last, axis, up)
        after = lax.ppermute(initial, axis, down)
        x = jnp.concatenate([before, x, after], axis=dim)
    return x


def band_table(kernel_taps, length_in, length_out, offset, forward):
    inner = lax.broadcasted_iota(jnp.int32, (length_in, length_out), 0)
    outer = lax.broadcasted_iota(jnp.int32, (length_in, length_out), 1)
    if forward:
        index_diff = inner - outer + offset
    else:
        index_diff = outer - inner + offset
    tap_ids = lax.broadcasted_iota(jnp.int32, (kernel_taps.shape[1], length_in, length_out), 0)
    onehot = (index_diff[None, :, :] == tap_ids).astype(jnp.float32)
    return jnp.einsum("rk,kio->rio", kernel_taps, onehot, precision=lax.Precision.HIGHEST)


def apply_blur(padded, axial_table, row_table, column_table):
    taps_in, span = axial_table.shape[1], padded.shape[1] * padded.shape[2]
    mixing = jnp.transpose(axial_table, (0, 2, 1)).reshape(-1, taps_in)
    flat = jnp.dot(mixing, padded.reshape(taps_in, span), precision=PREC)
    axial_pass = flat.reshape(axial_table.shape[0], axial_table.shape[2], padded.shape[1], padded.shape[2])
    row_pass = jnp.einsum("rwyx,ryv->rwvx", axial_pass, row_table, precision=PREC)
    return jnp.einsum("rwvx,rxu->wvu", row_pass, column_table, precision=PREC)


def widen(window, width, rows):
    return (max(0, window[0] - width), min(rows, window[1] + width))


def body(images, first_guess, axial_taps, row_taps, column_taps):
    recorded = images[0]
    planes, rows, columns = recorded.shape
    half = (axial_taps.shape[2] - 1) // 2
    margin = -(-half // 8) * 8
    view_count = lax.axis_size("view") * images.shape[0]
    axial, row_k, column_k = axial_taps[0], row_taps[0], column_taps[0]
    axial_fwd = band_table(axial, planes + 2 * half, planes, 0, True)
    axial_adj = band_table(axial, planes + 2 * half, planes, 2 * half, False)
    column_fwd = band_table(column_k, columns, columns, half, True)
    column_adj = band_table(column_k, columns, columns, half, False)
    pieces = PIECES if rows % (8 * PIECES) == 0 else 1
    step = rows // pieces
    needed = [[None] * (ITERS + 1) for _ in range(pieces)]
    for p in range(pieces):
        needed[p][ITERS] = (p * step, (p + 1) * step)
        for it in reversed(range(ITERS)):
            needed[p][it] = widen(needed[p][it + 1], 2 * margin, rows)
    made = [[(needed[p][0], None) for p in range(pieces)]]
    previous_log = None
    previous_sum = None
    for it in range(ITERS):
        made.append([])
        done_to = 0
        for p in range(pieces):
            target = needed[p][it + 1]
            ni, nj = (target[0], target[1]) if it + 1 == ITERS else (max(target[0], done_to), target[1])
            done_to = nj
            ri, rj = widen((ni, nj), margin, rows)
            ei, ej = widen((ri, rj), margin, rows)
            if it == 0:
                estimate = first_guess[:, ei:ej]
            else:
                parts = []
                for (ci, cj), values in made[it]:
                    lo, hi = max(ci, ei), min(cj, ej)
                    if lo < hi:
                        parts.append(values[:, lo - ci:hi - ci])
                estimate = jnp.concatenate(parts, axis=1) if len(parts) > 1 else parts[0]
            if previous_log is not None:
                estimate, _ = lax.optimization_barrier((estimate, previous_log))
            row_fwd = band_table(row_k, ej - ei, rj - ri, ei - ri + half, True)
            row_adj = band_table(row_k, rj - ri, nj - ni, ni - ri + half, False)
            padded_estimate = padded_2(estimate, (("gz", 0),), half)
            blurred = apply_blur(padded_estimate, axial_fwd, row_fwd, column_fwd)
            ratio = recorded[:, ri:rj] / blurred
            padded_ratio = padded_2(ratio, (("gz", 0),), half)
            correction = apply_blur(padded_ratio, axial_adj, row_adj, column_adj)
            log_terms = jnp.log(correction)
            previous_log = log_terms
            if previous_sum is not None:
                log_terms, _ = lax.optimization_barrier((log_terms, previous_sum))
            last = it + 1 == ITERS and p + 1 == pieces
            if planes % lax.axis_size("view") == 0 and log_terms.size >= (1 << 18) and not last:
                part_sum = lax.psum_scatter(log_terms, "view", scatter_dimension=0, tiled=True)
                logsum = lax.all_gather(part_sum, "view", axis=0, tiled=True)
            else:
                logsum = lax.psum(log_terms, "view")
            previous_sum = logsum
            updated = estimate[:, ni - ei:nj - ei] * jnp.exp(logsum / view_count)
            made[it + 1].append(((ni, nj), updated))
    outputs = [values for _, values in made[ITERS]]
    return jnp.concatenate(outputs, axis=1) if pieces > 1 else outputs[0]


def solution(mesh):
    in_specs = (
        P("view", ("tiles", "gz"), None, None),
        P(("tiles", "gz"), None, None),
        P("view", None, None),
        P("view", None, None),
        P("view", None, None),
    )
    out_specs = P(("tiles", "gz"), None, None)
    return jax.shard_map(body, mesh=mesh, in_specs=in_specs, out_specs=out_specs, check_vma=False)
```

```python
import jax
import jax.numpy as jnp
from jax import lax
from jax.sharding import PartitionSpec as P

ITERS = 2
PREC = lax.Precision.HIGH


def padded_2(x, sides, width):
    for axis, dim in sides:
        peers, length = (lax.axis_size(axis), x.shape[dim])
        up = [(i, (i + 1) % peers) for i in range(peers - 1)]
        down = [(j, i) for i, j in up]
        last = lax.slice_in_dim(x, length - width, length, axis=dim)
        initial = lax.slice_in_dim(x, 0, width, axis=dim)
        before = lax.ppermute(last, axis, up)
        after = lax.ppermute(initial, axis, down)
        x = jnp.concatenate([before, x, after], axis=dim)
    return x


def band_table(kernel_taps, length_in, length_out, offset, forward):
    inner = lax.broadcasted_iota(jnp.int32, (length_in, length_out), 0)
    outer = lax.broadcasted_iota(jnp.int32, (length_in, length_out), 1)
    if forward:
        index_diff = inner - outer + offset
    else:
        index_diff = outer - inner + offset
    tap_ids = lax.broadcasted_iota(jnp.int32, (kernel_taps.shape[1], length_in, length_out), 0)
    onehot = (index_diff[None, :, :] == tap_ids).astype(jnp.float32)
    return jnp.einsum("rk,kio->rio", kernel_taps, onehot, precision=lax.Precision.HIGHEST)


def apply_blur(padded, axial_table, row_table, column_table):
    taps_in, span = axial_table.shape[1], padded.shape[1] * padded.shape[2]
    mixing = jnp.transpose(axial_table, (0, 2, 1)).reshape(-1, taps_in)
    flat = jnp.dot(mixing, padded.reshape(taps_in, span), precision=PREC)
    axial_pass = flat.reshape(axial_table.shape[0], axial_table.shape[2], padded.shape[1], padded.shape[2])
    row_pass = jnp.einsum("rwyx,ryv->rwvx", axial_pass, row_table, precision=PREC)
    return jnp.einsum("rwvx,rxu->wvu", row_pass, column_table, precision=PREC)


def widen(window, width, rows):
    return (max(0, window[0] - width), min(rows, window[1] + width))


def body(images, first_guess, axial_taps, row_taps, column_taps):
    recorded = images[0]
    planes, rows, columns = recorded.shape
    half = (axial_taps.shape[2] - 1) // 2
    margin = -(-half // 8) * 8
    view_count = lax.axis_size("view") * images.shape[0]
    axial, row_k, column_k = axial_taps[0], row_taps[0], column_taps[0]
    axial_fwd = band_table(axial, planes + 2 * half, planes, 0, True)
    axial_adj = band_table(axial, planes + 2 * half, planes, 2 * half, False)
    column_fwd = band_table(column_k, columns, columns, half, True)
    column_adj = band_table(column_k, columns, columns, half, False)
    half_rows = rows // 2
    if rows % 16 == 0 and ITERS >= 2:
        last_parts = [(0, half_rows), (half_rows, rows)]
        reach = min(rows, half_rows + 2 * margin)
        cut = (reach // 2) // 8 * 8
        early_parts = [(0, rows)]
    else:
        last_parts = early_parts = [(0, rows)]
    partitions = [early_parts if it + 2 == ITERS else ([(0, rows)] if it + 1 < ITERS else last_parts)
                  for it in range(ITERS)]
    made = [[((0, rows), first_guess)]]
    previous_log = None
    previous_sum = None
    for it in range(ITERS):
        made.append([])
        for index, (ni, nj) in enumerate(partitions[it]):
            ri, rj = widen((ni, nj), margin, rows)
            ei, ej = widen((ri, rj), margin, rows)
            parts = []
            for (ci, cj), values in made[it]:
                lo, hi = max(ci, ei), min(cj, ej)
                if lo < hi:
                    parts.append(values[:, lo - ci:hi - ci])
            estimate = jnp.concatenate(parts, axis=1) if len(parts) > 1 else parts[0]
            if previous_log is not None:
                estimate, _ = lax.optimization_barrier((estimate, previous_log))
            row_fwd = band_table(row_k, ej - ei, rj - ri, ei - ri + half, True)
            row_adj = band_table(row_k, rj - ri, nj - ni, ni - ri + half, False)
            padded_estimate = padded_2(estimate, (("gz", 0),), half)
            blurred = apply_blur(padded_estimate, axial_fwd, row_fwd, column_fwd)
            ratio = recorded[:, ri:rj] / blurred
            padded_ratio = padded_2(ratio, (("gz", 0),), half)
            correction = apply_blur(padded_ratio, axial_adj, row_adj, column_adj)
            log_terms = jnp.log(correction)
            previous_log = log_terms
            if previous_sum is not None:
                log_terms, _ = lax.optimization_barrier((log_terms, previous_sum))
            last = it + 1 == ITERS and index + 1 == len(partitions[it])
            alone = len(partitions[it]) == 1
            if planes % lax.axis_size("view") == 0 and log_terms.size >= (1 << 18) and not last and not alone:
                part_sum = lax.psum_scatter(log_terms, "view", scatter_dimension=0, tiled=True)
                logsum = lax.all_gather(part_sum, "view", axis=0, tiled=True)
            else:
                logsum = lax.psum(log_terms, "view")
            previous_sum = logsum
            updated = estimate[:, ni - ei:nj - ei] * jnp.exp(logsum / view_count)
            made[it + 1].append(((ni, nj), updated))
    outputs = [values for _, values in made[ITERS]]
    return jnp.concatenate(outputs, axis=1) if len(outputs) > 1 else outputs[0]


def solution(mesh):
    in_specs = (
        P("view", ("tiles", "gz"), None, None),
        P(("tiles", "gz"), None, None),
        P("view", None, None),
        P("view", None, None),
        P("view", None, None),
    )
    out_specs = P(("tiles", "gz"), None, None)
    return jax.shard_map(body, mesh=mesh, in_specs=in_specs, out_specs=out_specs, check_vma=False)
```

```python
import jax
import jax.numpy as jnp
from jax import lax
from jax.sharding import PartitionSpec as P

ITERS = 2
PREC = lax.Precision.HIGH
PIECES = 2


def padded_2(x, sides, width):
    for axis, dim in sides:
        peers, length = (lax.axis_size(axis), x.shape[dim])
        up = [(i, (i + 1) % peers) for i in range(peers - 1)]
        down = [(j, i) for i, j in up]
        last = lax.slice_in_dim(x, length - width, length, axis=dim)
        initial = lax.slice_in_dim(x, 0, width, axis=dim)
        before = lax.ppermute(last, axis, up)
        after = lax.ppermute(initial, axis, down)
        x = jnp.concatenate([before, x, after], axis=dim)
    return x


def band_table(kernel_taps, length_in, length_out, offset, forward):
    inner = lax.broadcasted_iota(jnp.int32, (length_in, length_out), 0)
    outer = lax.broadcasted_iota(jnp.int32, (length_in, length_out), 1)
    if forward:
        index_diff = inner - outer + offset
    else:
        index_diff = outer - inner + offset
    tap_ids = lax.broadcasted_iota(jnp.int32, (kernel_taps.shape[1], length_in, length_out), 0)
    onehot = (index_diff[None, :, :] == tap_ids).astype(jnp.float32)
    return jnp.einsum("rk,kio->rio", kernel_taps, onehot, precision=lax.Precision.HIGHEST)


def apply_blur(padded, axial_table, row_table, column_table):
    taps_in, span = axial_table.shape[1], padded.shape[1] * padded.shape[2]
    mixing = jnp.transpose(axial_table, (0, 2, 1)).reshape(-1, taps_in)
    flat = jnp.dot(mixing, padded.reshape(taps_in, span), precision=PREC)
    axial_pass = flat.reshape(axial_table.shape[0], axial_table.shape[2], padded.shape[1], padded.shape[2])
    row_pass = jnp.einsum("rwyx,ryv->rwvx", axial_pass, row_table, precision=PREC)
    return jnp.einsum("rwvx,rxu->wvu", row_pass, column_table, precision=PREC)


def widen(window, width, rows):
    return (max(0, window[0] - width), min(rows, window[1] + width))


def body(images, first_guess, axial_taps, row_taps, column_taps):
    recorded = images[0]
    planes, rows, columns = recorded.shape
    half = (axial_taps.shape[2] - 1) // 2
    margin = -(-half // 8) * 8
    view_count = lax.axis_size("view") * images.shape[0]
    axial, row_k, column_k = axial_taps[0], row_taps[0], column_taps[0]
    axial_fwd = band_table(axial, planes + 2 * half, planes, 0, True)
    axial_adj = band_table(axial, planes + 2 * half, planes, 2 * half, False)
    column_fwd = band_table(column_k, columns, columns, half, True)
    column_adj = band_table(column_k, columns, columns, half, False)
    pieces = PIECES if rows % (8 * PIECES) == 0 else 1
    step = rows // pieces
    needed = [[None] * (ITERS + 1) for _ in range(pieces)]
    for p in range(pieces):
        needed[p][ITERS] = (p * step, (p + 1) * step)
        for it in reversed(range(ITERS)):
            needed[p][it] = widen(needed[p][it + 1], 2 * margin, rows)
    made = [[(needed[p][0], None) for p in range(pieces)]]
    previous_log = None
    previous_sum = None
    pending = None

    def finish(target, logsum, held):
        values, window = held
        target.append((window, values * jnp.exp(logsum / view_count)))

    for it in range(ITERS):
        made.append([])
        done_to = 0
        for p in range(pieces):
            target = needed[p][it + 1]
            ni, nj = (target[0], target[1]) if it + 1 == ITERS else (max(target[0], done_to), target[1])
            done_to = nj
            ri, rj = widen((ni, nj), margin, rows)
            ei, ej = widen((ri, rj), margin, rows)
            if it == 0:
                estimate = first_guess[:, ei:ej]
            else:
                parts = []
                for (ci, cj), values in made[it]:
                    lo, hi = max(ci, ei), min(cj, ej)
                    if lo < hi:
                        parts.append(values[:, lo - ci:hi - ci])
                estimate = jnp.concatenate(parts, axis=1) if len(parts) > 1 else parts[0]
            if previous_log is not None:
                estimate, _ = lax.optimization_barrier((estimate, previous_log))
            row_fwd = band_table(row_k, ej - ei, rj - ri, ei - ri + half, True)
            row_adj = band_table(row_k, rj - ri, nj - ni, ni - ri + half, False)
            padded_estimate = padded_2(estimate, (("gz", 0),), half)
            blurred = apply_blur(padded_estimate, axial_fwd, row_fwd, column_fwd)
            ratio = recorded[:, ri:rj] / blurred
            padded_ratio = padded_2(ratio, (("gz", 0),), half)
            correction = apply_blur(padded_ratio, axial_adj, row_adj, column_adj)
            log_terms = jnp.log(correction)
            previous_log = log_terms
            if previous_sum is not None:
                log_terms, _ = lax.optimization_barrier((log_terms, previous_sum))
            last = it + 1 == ITERS and p + 1 == pieces
            if planes % lax.axis_size("view") == 0 and log_terms.size >= (1 << 18) and not last:
                part_sum = lax.psum_scatter(log_terms, "view", scatter_dimension=0, tiled=True)
                logsum = lax.all_gather(part_sum, "view", axis=0, tiled=True)
            else:
                logsum = lax.psum(log_terms, "view")
            previous_sum = logsum
            if pending is not None:
                tied, _ = lax.optimization_barrier((pending[1], log_terms))
                finish(pending[0], tied, pending[2])
            pending = (made[it + 1], logsum, (estimate[:, ni - ei:nj - ei], (ni, nj)))
    finish(pending[0], pending[1], pending[2])
    outputs = [values for _, values in made[ITERS]]
    return jnp.concatenate(outputs, axis=1) if pieces > 1 else outputs[0]


def solution(mesh):
    in_specs = (
        P("view", ("tiles", "gz"), None, None),
        P(("tiles", "gz"), None, None),
        P("view", None, None),
        P("view", None, None),
        P("view", None, None),
    )
    out_specs = P(("tiles", "gz"), None, None)
    return jax.shard_map(body, mesh=mesh, in_specs=in_specs, out_specs=out_specs, check_vma=False)
```

```python
import jax
import jax.numpy as jnp
from jax import lax
from jax.sharding import PartitionSpec as P

ITERS = 2
PREC = lax.Precision.HIGH
PIECES = 2


def padded_2(x, sides, width):
    for axis, dim in sides:
        peers, length = (lax.axis_size(axis), x.shape[dim])
        up = [(i, (i + 1) % peers) for i in range(peers - 1)]
        down = [(j, i) for i, j in up]
        last = lax.slice_in_dim(x, length - width, length, axis=dim)
        initial = lax.slice_in_dim(x, 0, width, axis=dim)
        before = lax.ppermute(last, axis, up)
        after = lax.ppermute(initial, axis, down)
        x = jnp.concatenate([before, x, after], axis=dim)
    return x


def band_table(kernel_taps, length_in, length_out, offset, forward):
    inner = lax.broadcasted_iota(jnp.int32, (length_in, length_out), 0)
    outer = lax.broadcasted_iota(jnp.int32, (length_in, length_out), 1)
    if forward:
        index_diff = inner - outer + offset
    else:
        index_diff = outer - inner + offset
    tap_ids = lax.broadcasted_iota(jnp.int32, (kernel_taps.shape[1], length_in, length_out), 0)
    onehot = (index_diff[None, :, :] == tap_ids).astype(jnp.float32)
    return jnp.einsum("rk,kio->rio", kernel_taps, onehot, precision=lax.Precision.HIGHEST)


def apply_blur(padded, axial_table, row_table, column_table):
    taps_in, span = axial_table.shape[1], padded.shape[1] * padded.shape[2]
    mixing = jnp.transpose(axial_table, (0, 2, 1)).reshape(-1, taps_in)
    flat = jnp.dot(mixing, padded.reshape(taps_in, span), precision=PREC)
    axial_pass = flat.reshape(axial_table.shape[0], axial_table.shape[2], padded.shape[1], padded.shape[2])
    row_pass = jnp.einsum("rwyx,ryv->rwvx", axial_pass, row_table, precision=PREC)
    return jnp.einsum("rwvx,rxu->wvu", row_pass, column_table, precision=PREC)


def widen(window, width, rows):
    return (max(0, window[0] - width), min(rows, window[1] + width))


def body(images, first_guess, axial_taps, row_taps, column_taps):
    recorded = images[0]
    planes, rows, columns = recorded.shape
    half = (axial_taps.shape[2] - 1) // 2
    margin = -(-half // 8) * 8
    view_count = lax.axis_size("view") * images.shape[0]
    axial, row_k, column_k = axial_taps[0], row_taps[0], column_taps[0]
    axial_fwd = band_table(axial, planes + 2 * half, planes, 0, True)
    axial_adj = band_table(axial, planes + 2 * half, planes, 2 * half, False)
    column_fwd = band_table(column_k, columns, columns, half, True)
    column_adj = band_table(column_k, columns, columns, half, False)
    pieces = PIECES if rows % (8 * PIECES) == 0 else 1
    step = rows // pieces
    split = (step - 2 * margin) // 8 * 8 if pieces == 2 else 0
    if split <= 0:
        split = step
    bounds = [(0, split), (split, rows)] if pieces == 2 else [(0, rows)]
    needed = [[None] * (ITERS + 1) for _ in range(pieces)]
    for p in range(pieces):
        needed[p][ITERS] = bounds[p]
        for it in reversed(range(ITERS)):
            needed[p][it] = widen(needed[p][it + 1], 2 * margin, rows)
    made = [[(needed[p][0], None) for p in range(pieces)]]
    previous_log = None
    previous_sum = None
    for it in range(ITERS):
        made.append([])
        done_to = 0
        for p in range(pieces):
            target = needed[p][it + 1]
            ni, nj = (target[0], target[1]) if it + 1 == ITERS else (max(target[0], done_to), target[1])
            done_to = nj
            ri, rj = widen((ni, nj), margin, rows)
            ei, ej = widen((ri, rj), margin, rows)
            if it == 0:
                estimate = first_guess[:, ei:ej]
            else:
                parts = []
                for (ci, cj), values in made[it]:
                    lo, hi = max(ci, ei), min(cj, ej)
                    if lo < hi:
                        parts.append(values[:, lo - ci:hi - ci])
                estimate = jnp.concatenate(parts, axis=1) if len(parts) > 1 else parts[0]
            if previous_log is not None:
                estimate, _ = lax.optimization_barrier((estimate, previous_log))
            row_fwd = band_table(row_k, ej - ei, rj - ri, ei - ri + half, True)
            row_adj = band_table(row_k, rj - ri, nj - ni, ni - ri + half, False)
            padded_estimate = padded_2(estimate, (("gz", 0),), half)
            blurred = apply_blur(padded_estimate, axial_fwd, row_fwd, column_fwd)
            ratio = recorded[:, ri:rj] / blurred
            padded_ratio = padded_2(ratio, (("gz", 0),), half)
            correction = apply_blur(padded_ratio, axial_adj, row_adj, column_adj)
            log_terms = jnp.log(correction)
            previous_log = log_terms
            if previous_sum is not None:
                log_terms, _ = lax.optimization_barrier((log_terms, previous_sum))
            last = it + 1 == ITERS and p + 1 == pieces
            if planes % lax.axis_size("view") == 0 and log_terms.size >= (1 << 18) and not last:
                part_sum = lax.psum_scatter(log_terms, "view", scatter_dimension=0, tiled=True)
                logsum = lax.all_gather(part_sum, "view", axis=0, tiled=True)
            else:
                logsum = lax.psum(log_terms, "view")
            previous_sum = logsum
            updated = estimate[:, ni - ei:nj - ei] * jnp.exp(logsum / view_count)
            made[it + 1].append(((ni, nj), updated))
    outputs = [values for _, values in made[ITERS]]
    return jnp.concatenate(outputs, axis=1) if pieces > 1 else outputs[0]


def solution(mesh):
    in_specs = (
        P("view", ("tiles", "gz"), None, None),
        P(("tiles", "gz"), None, None),
        P("view", None, None),
        P("view", None, None),
        P("view", None, None),
    )
    out_specs = P(("tiles", "gz"), None, None)
    return jax.shard_map(body, mesh=mesh, in_specs=in_specs, out_specs=out_specs, check_vma=False)
```

```python
import jax
import jax.numpy as jnp
from jax import lax
from jax.sharding import PartitionSpec as P

ITERS = 2
PREC = lax.Precision.HIGH
PIECES = 2


def padded_2(x, sides, width):
    for axis, dim in sides:
        peers, length = (lax.axis_size(axis), x.shape[dim])
        up = [(i, (i + 1) % peers) for i in range(peers - 1)]
        down = [(j, i) for i, j in up]
        last = lax.slice_in_dim(x, length - width, length, axis=dim)
        initial = lax.slice_in_dim(x, 0, width, axis=dim)
        before = lax.ppermute(last, axis, up)
        after = lax.ppermute(initial, axis, down)
        x = jnp.concatenate([before, x, after], axis=dim)
    return x


def band_table(kernel_taps, length_in, length_out, offset, forward):
    inner = lax.broadcasted_iota(jnp.int32, (length_in, length_out), 0)
    outer = lax.broadcasted_iota(jnp.int32, (length_in, length_out), 1)
    if forward:
        index_diff = inner - outer + offset
    else:
        index_diff = outer - inner + offset
    tap_ids = lax.broadcasted_iota(jnp.int32, (kernel_taps.shape[1], length_in, length_out), 0)
    onehot = (index_diff[None, :, :] == tap_ids).astype(jnp.float32)
    return jnp.einsum("rk,kio->rio", kernel_taps, onehot, precision=lax.Precision.HIGHEST)


def apply_blur(padded, axial_table, row_table, column_table):
    taps_in, span = axial_table.shape[1], padded.shape[1] * padded.shape[2]
    mixing = jnp.transpose(axial_table, (0, 2, 1)).reshape(-1, taps_in)
    flat = jnp.dot(mixing, padded.reshape(taps_in, span), precision=PREC)
    axial_pass = flat.reshape(axial_table.shape[0], axial_table.shape[2], padded.shape[1], padded.shape[2])
    row_pass = jnp.einsum("rwyx,ryv->rwvx", axial_pass, row_table, precision=PREC)
    return jnp.einsum("rwvx,rxu->wvu", row_pass, column_table, precision=PREC)


def widen(window, width, rows):
    return (max(0, window[0] - width), min(rows, window[1] + width))


def body(images, first_guess, axial_taps, row_taps, column_taps):
    recorded = images[0]
    planes, rows, columns = recorded.shape
    half = (axial_taps.shape[2] - 1) // 2
    margin = -(-half // 8) * 8
    view_count = lax.axis_size("view") * images.shape[0]
    axial, row_k, column_k = axial_taps[0], row_taps[0], column_taps[0]
    axial_fwd = band_table(axial, planes + 2 * half, planes, 0, True)
    axial_adj = band_table(axial, planes + 2 * half, planes, 2 * half, False)
    column_fwd = band_table(column_k, columns, columns, half, True)
    column_adj = band_table(column_k, columns, columns, half, False)
    pieces = PIECES if rows % (8 * PIECES) == 0 else 1
    step = rows // pieces
    needed = [[None] * (ITERS + 1) for _ in range(pieces)]
    for p in range(pieces):
        needed[p][ITERS] = (p * step, (p + 1) * step)
        for it in reversed(range(ITERS)):
            needed[p][it] = widen(needed[p][it + 1], 2 * margin, rows)
    made = [[(needed[p][0], None) for p in range(pieces)]]
    previous_log = None
    previous_sum = None
    for it in range(ITERS):
        made.append([])
        done_to = 0
        fill_rows = -(-(1 << 18) // (planes * columns * 8)) * 8
        for p in range(pieces):
            target = needed[p][it + 1]
            ni, nj = (target[0], target[1]) if it + 1 == ITERS else (max(target[0], done_to), target[1])
            if it + 1 < ITERS and nj - ni < fill_rows:
                ni = max(target[0], nj - fill_rows)
            done_to = nj
            ri, rj = widen((ni, nj), margin, rows)
            ei, ej = widen((ri, rj), margin, rows)
            if it == 0:
                estimate = first_guess[:, ei:ej]
            else:
                parts = []
                cursor = ei
                for (ci, cj), values in made[it]:
                    lo, hi = max(ci, cursor), min(cj, ej)
                    if lo < hi:
                        parts.append(values[:, lo - ci:hi - ci])
                        cursor = hi
                estimate = jnp.concatenate(parts, axis=1) if len(parts) > 1 else parts[0]
            if previous_log is not None:
                estimate, _ = lax.optimization_barrier((estimate, previous_log))
            row_fwd = band_table(row_k, ej - ei, rj - ri, ei - ri + half, True)
            row_adj = band_table(row_k, rj - ri, nj - ni, ni - ri + half, False)
            padded_estimate = padded_2(estimate, (("gz", 0),), half)
            blurred = apply_blur(padded_estimate, axial_fwd, row_fwd, column_fwd)
            ratio = recorded[:, ri:rj] / blurred
            padded_ratio = padded_2(ratio, (("gz", 0),), half)
            correction = apply_blur(padded_ratio, axial_adj, row_adj, column_adj)
            log_terms = jnp.log(correction)
            previous_log = log_terms
            if previous_sum is not None:
                log_terms, _ = lax.optimization_barrier((log_terms, previous_sum))
            last = it + 1 == ITERS and p + 1 == pieces
            if planes % lax.axis_size("view") == 0 and log_terms.size >= (1 << 18) and not last:
                part_sum = lax.psum_scatter(log_terms, "view", scatter_dimension=0, tiled=True)
                logsum = lax.all_gather(part_sum, "view", axis=0, tiled=True)
            else:
                logsum = lax.psum(log_terms, "view")
            previous_sum = logsum
            updated = estimate[:, ni - ei:nj - ei] * jnp.exp(logsum / view_count)
            made[it + 1].append(((ni, nj), updated))
    outputs = [values for _, values in made[ITERS]]
    return jnp.concatenate(outputs, axis=1) if pieces > 1 else outputs[0]


def solution(mesh):
    in_specs = (
        P("view", ("tiles", "gz"), None, None),
        P(("tiles", "gz"), None, None),
        P("view", None, None),
        P("view", None, None),
        P("view", None, None),
    )
    out_specs = P(("tiles", "gz"), None, None)
    return jax.shard_map(body, mesh=mesh, in_specs=in_specs, out_specs=out_specs, check_vma=False)
```

```python
import jax
import jax.numpy as jnp
from jax import lax
from jax.sharding import PartitionSpec as P

ITERS = 2
PREC = lax.Precision.HIGH
PIECES = 2


def padded_2(x, sides, width):
    for axis, dim in sides:
        peers, length = (lax.axis_size(axis), x.shape[dim])
        up = [(i, (i + 1) % peers) for i in range(peers - 1)]
        down = [(j, i) for i, j in up]
        last = lax.slice_in_dim(x, length - width, length, axis=dim)
        initial = lax.slice_in_dim(x, 0, width, axis=dim)
        before = lax.ppermute(last, axis, up)
        after = lax.ppermute(initial, axis, down)
        x = jnp.concatenate([before, x, after], axis=dim)
    return x


def band_table(kernel_taps, length_in, length_out, offset, forward):
    inner = lax.broadcasted_iota(jnp.int32, (length_in, length_out), 0)
    outer = lax.broadcasted_iota(jnp.int32, (length_in, length_out), 1)
    if forward:
        index_diff = inner - outer + offset
    else:
        index_diff = outer - inner + offset
    tap_ids = lax.broadcasted_iota(jnp.int32, (kernel_taps.shape[1], length_in, length_out), 0)
    onehot = (index_diff[None, :, :] == tap_ids).astype(jnp.float32)
    return jnp.einsum("rk,kio->rio", kernel_taps, onehot, precision=lax.Precision.HIGHEST)


def apply_blur(padded, axial_table, row_table, column_table):
    taps_in, span = axial_table.shape[1], padded.shape[1] * padded.shape[2]
    mixing = jnp.transpose(axial_table, (0, 2, 1)).reshape(-1, taps_in)
    flat = jnp.dot(mixing, padded.reshape(taps_in, span), precision=PREC)
    axial_pass = flat.reshape(axial_table.shape[0], axial_table.shape[2], padded.shape[1], padded.shape[2])
    row_pass = jnp.einsum("rwyx,ryv->rwvx", axial_pass, row_table, precision=PREC)
    return jnp.einsum("rwvx,rxu->wvu", row_pass, column_table, precision=PREC)


def widen(window, width, rows):
    return (max(0, window[0] - width), min(rows, window[1] + width))


def body(images, first_guess, axial_taps, row_taps, column_taps):
    recorded = images[0]
    planes, rows, columns = recorded.shape
    half = (axial_taps.shape[2] - 1) // 2
    margin = -(-half // 8) * 8
    view_count = lax.axis_size("view") * images.shape[0]
    axial, row_k, column_k = axial_taps[0], row_taps[0], column_taps[0]
    axial_fwd = band_table(axial, planes + 2 * half, planes, 0, True)
    axial_adj = band_table(axial, planes + 2 * half, planes, 2 * half, False)
    column_fwd = band_table(column_k, columns, columns, half, True)
    column_adj = band_table(column_k, columns, columns, half, False)
    pieces = PIECES if rows % (8 * PIECES) == 0 else 1
    step = rows // pieces
    needed = [[None] * (ITERS + 1) for _ in range(pieces)]
    for p in range(pieces):
        needed[p][ITERS] = (p * step, (p + 1) * step)
        for it in reversed(range(ITERS)):
            needed[p][it] = widen(needed[p][it + 1], 2 * margin, rows)
    made = [[(needed[p][0], None) for p in range(pieces)]]
    previous_log = None
    previous_sum = None
    for it in range(ITERS):
        made.append([])
        done_to = 0
        for p in range(pieces):
            target = needed[p][it + 1]
            ni, nj = (target[0], target[1]) if it + 1 == ITERS else (max(target[0], done_to), target[1])
            done_to = nj
            ri, rj = widen((ni, nj), margin, rows)
            ei, ej = widen((ri, rj), margin, rows)
            if it == 0:
                estimate = first_guess[:, ei:ej]
            else:
                parts = []
                for (ci, cj), values in made[it]:
                    lo, hi = max(ci, ei), min(cj, ej)
                    if lo < hi:
                        parts.append(values[:, lo - ci:hi - ci])
                estimate = jnp.concatenate(parts, axis=1) if len(parts) > 1 else parts[0]
            if previous_log is not None:
                estimate, _ = lax.optimization_barrier((estimate, previous_log))
            row_fwd = band_table(row_k, ej - ei, rj - ri, ei - ri + half, True)
            row_adj = band_table(row_k, rj - ri, nj - ni, ni - ri + half, False)
            padded_estimate = padded_2(estimate, (("gz", 0),), half)
            blurred = apply_blur(padded_estimate, axial_fwd, row_fwd, column_fwd)
            ratio = recorded[:, ri:rj] / blurred
            padded_ratio = padded_2(ratio, (("gz", 0),), half)
            correction = apply_blur(padded_ratio, axial_adj, row_adj, column_adj)
            log_terms = jnp.log(correction)
            previous_log = log_terms
            if previous_sum is not None:
                log_terms, _ = lax.optimization_barrier((log_terms, previous_sum))
            last = it + 1 == ITERS and p + 1 == pieces
            if planes % lax.axis_size("view") == 0 and log_terms.size >= (1 << 18) and not last and it == 0:
                part_sum = lax.psum_scatter(log_terms, "view", scatter_dimension=0, tiled=True)
                logsum = lax.all_gather(part_sum, "view", axis=0, tiled=True)
            else:
                logsum = lax.psum(log_terms, "view")
            previous_sum = logsum
            updated = estimate[:, ni - ei:nj - ei] * jnp.exp(logsum / view_count)
            made[it + 1].append(((ni, nj), updated))
    outputs = [values for _, values in made[ITERS]]
    return jnp.concatenate(outputs, axis=1) if pieces > 1 else outputs[0]


def solution(mesh):
    in_specs = (
        P("view", ("tiles", "gz"), None, None),
        P(("tiles", "gz"), None, None),
        P("view", None, None),
        P("view", None, None),
        P("view", None, None),
    )
    out_specs = P(("tiles", "gz"), None, None)
    return jax.shard_map(body, mesh=mesh, in_specs=in_specs, out_specs=out_specs, check_vma=False)
```

```python
import jax
import jax.numpy as jnp
from jax import lax
from jax.sharding import PartitionSpec as P

ITERS = 2
PREC = lax.Precision.HIGH
PIECES = 2


def padded_2(x, sides, width):
    for axis, dim in sides:
        peers, length = (lax.axis_size(axis), x.shape[dim])
        up = [(i, (i + 1) % peers) for i in range(peers - 1)]
        down = [(j, i) for i, j in up]
        last = lax.slice_in_dim(x, length - width, length, axis=dim)
        initial = lax.slice_in_dim(x, 0, width, axis=dim)
        before = lax.ppermute(last, axis, up)
        after = lax.ppermute(initial, axis, down)
        x = jnp.concatenate([before, x, after], axis=dim)
    return x


def band_table(kernel_taps, length_in, length_out, offset, forward):
    inner = lax.broadcasted_iota(jnp.int32, (length_in, length_out), 0)
    outer = lax.broadcasted_iota(jnp.int32, (length_in, length_out), 1)
    if forward:
        index_diff = inner - outer + offset
    else:
        index_diff = outer - inner + offset
    tap_ids = lax.broadcasted_iota(jnp.int32, (kernel_taps.shape[1], length_in, length_out), 0)
    onehot = (index_diff[None, :, :] == tap_ids).astype(jnp.float32)
    return jnp.einsum("rk,kio->rio", kernel_taps, onehot, precision=lax.Precision.HIGHEST)


def apply_blur(padded, axial_table, row_table, column_table):
    taps_in, span = axial_table.shape[1], padded.shape[1] * padded.shape[2]
    mixing = jnp.transpose(axial_table, (0, 2, 1)).reshape(-1, taps_in)
    flat = jnp.dot(mixing, padded.reshape(taps_in, span), precision=PREC)
    axial_pass = flat.reshape(axial_table.shape[0], axial_table.shape[2], padded.shape[1], padded.shape[2])
    row_pass = jnp.einsum("rwyx,ryv->rwvx", axial_pass, row_table, precision=PREC)
    return jnp.einsum("rwvx,rxu->wvu", row_pass, column_table, precision=PREC)


def widen(window, width, rows):
    return (max(0, window[0] - width), min(rows, window[1] + width))


def body(images, first_guess, axial_taps, row_taps, column_taps):
    recorded = images[0]
    planes, rows, columns = recorded.shape
    half = (axial_taps.shape[2] - 1) // 2
    margin = -(-half // 8) * 8
    view_count = lax.axis_size("view") * images.shape[0]
    axial, row_k, column_k = axial_taps[0], row_taps[0], column_taps[0]
    axial_fwd = band_table(axial, planes + 2 * half, planes, 0, True)
    axial_adj = band_table(axial, planes + 2 * half, planes, 2 * half, False)
    column_fwd = band_table(column_k, columns, columns, half, True)
    column_adj = band_table(column_k, columns, columns, half, False)
    pieces = PIECES if rows % (8 * PIECES) == 0 else 1
    step = rows // pieces
    needed = [[None] * (ITERS + 1) for _ in range(pieces)]
    for p in range(pieces):
        needed[p][ITERS] = (p * step, (p + 1) * step)
        for it in reversed(range(ITERS)):
            needed[p][it] = widen(needed[p][it + 1], 2 * margin, rows)
    made = [[(needed[p][0], None) for p in range(pieces)]]
    previous_log = None
    previous_sum = None
    for it in range(ITERS):
        made.append([])
        done_to = 0
        for p in range(pieces):
            target = needed[p][it + 1]
            ni, nj = (target[0], target[1]) if it + 1 == ITERS else (max(target[0], done_to), target[1])
            done_to = nj
            ri, rj = widen((ni, nj), margin, rows)
            ei, ej = widen((ri, rj), margin, rows)
            if it == 0:
                estimate = first_guess[:, ei:ej]
            else:
                parts = []
                for (ci, cj), values in made[it]:
                    lo, hi = max(ci, ei), min(cj, ej)
                    if lo < hi:
                        parts.append(values[:, lo - ci:hi - ci])
                estimate = jnp.concatenate(parts, axis=1) if len(parts) > 1 else parts[0]
            if previous_log is not None:
                estimate, _ = lax.optimization_barrier((estimate, previous_log))
            row_fwd = band_table(row_k, ej - ei, rj - ri, ei - ri + half, True)
            row_adj = band_table(row_k, rj - ri, nj - ni, ni - ri + half, False)
            padded_estimate = padded_2(estimate, (("gz", 0),), half)
            blurred = apply_blur(padded_estimate, axial_fwd, row_fwd, column_fwd)
            ratio = recorded[:, ri:rj] / blurred
            padded_ratio = padded_2(ratio, (("gz", 0),), half)
            correction = apply_blur(padded_ratio, axial_adj, row_adj, column_adj)
            log_terms = jnp.log(correction)
            previous_log = log_terms
            if previous_sum is not None:
                log_terms, _ = lax.optimization_barrier((log_terms, previous_sum))
            last = it + 1 == ITERS and p + 1 == pieces
            if planes % lax.axis_size("view") == 0 and log_terms.size >= (1 << 18) and not last:
                part_sum = lax.psum_scatter(log_terms, "view", scatter_dimension=0, tiled=True)
                logsum = lax.all_gather(part_sum, "view", axis=0, tiled=True)
            else:
                logsum = lax.psum(log_terms, "view")
            previous_sum = logsum
            held = estimate[:, ni - ei:nj - ei]
            if last and pieces > 1:
                final_part = (held, logsum)
            else:
                made[it + 1].append(((ni, nj), held * jnp.exp(logsum / view_count)))
    if pieces == 1:
        return made[ITERS][0][1]
    held, logsum = final_part
    values = jnp.concatenate([v for _, v in made[ITERS]] + [held], axis=1)
    ones = jnp.ones(values.shape[:1] + (values.shape[1] - held.shape[1],) + values.shape[2:], jnp.float32)
    scale = jnp.concatenate([ones, jnp.exp(logsum / view_count)], axis=1)
    return values * scale


def solution(mesh):
    in_specs = (
        P("view", ("tiles", "gz"), None, None),
        P(("tiles", "gz"), None, None),
        P("view", None, None),
        P("view", None, None),
        P("view", None, None),
    )
    out_specs = P(("tiles", "gz"), None, None)
    return jax.shard_map(body, mesh=mesh, in_specs=in_specs, out_specs=out_specs, check_vma=False)
```
